256 devices in a mesh: row: 32 (over z, y), col: 8 (over x, core).
Axes of the slice: x: 4, y: 4, z: 8, core: 2. Of those that a mesh axis runs over, the one named last changes fastest.
Arguments:
- saved_input: bfloat16 [1024, 49152], P('col', 'row'), may hold values from -6 to 6
- out_grad: bfloat16 [1024, 12288], P('row', 'col'), may hold values from -0.75 to 0.75
- weight: bfloat16 [49152, 12288], P('row', 'col'), may hold values from -0.625 to 0.625
Outputs:
- in_grad: bfloat16 [1024, 49152], P('col', 'row')
- weight_grad: bfloat16 [49152, 12288], P('row', 'col')
The draws below stay inside these ranges and needn't reach their ends.
All inputs are finite; a program needn't handle non-finite values.
Results may differ from the reference program's by a relative error of at most 0.0051.
Values may be sent and summed in bfloat16 or wider, within the bound.
No kernel may reach another device: no remote copies, remote signals or barrier semaphores. Data moves between devices by JAX's collectives and lax.ppermute only.
A program may use at most 64 MiB of HBM per device.

```python
import math
import jax
import jax.numpy as jnp
from jax import lax

D = 12288
H = 49152
TOKENS = 1024


def raised(array, key, source, target, parts, factor):
    owner, partner = [(jnp.arange(array.shape[axis_at]) // (array.shape[axis_at] // parts)).reshape([-1 if axis == axis_at else 1 for axis in range(array.ndim)]) for axis_at in (source, target)]
    chosen = jax.random.permutation(key, parts)[partner]
    strong = (owner == chosen) | (owner == (partner + parts // 2) % parts)
    return jnp.where(strong, factor * array, array)


def block_levels(rng, extent, shards, least, top_value):
    factor_of = 1.0
    for axis_at, blocks in shards:
        draws = jax.random.uniform(jax.random.fold_in(jax.random.fold_in(rng, 6), axis_at), (blocks,), jnp.float32, least / len(shards), top_value / len(shards))
        factor_of = factor_of * jnp.repeat(jnp.exp(draws), extent[axis_at] // blocks).reshape((-1,) + (1,) * (len(extent) - 1 - axis_at))
    return factor_of


def noise(key, shape, scale, reach, shards=(), held_as=jnp.bfloat16):
    result = scale * jax.random.normal(key, shape, jnp.float32)
    if shards:
        result = result * block_levels(key, shape, shards, -0.22, 0.18)
    return jnp.clip(result, -reach, reach).astype(held_as)


def gaussian_with(stream_key, shape, width, limit, cuts, heavy, kind=jnp.bfloat16):
    drawn = width * jax.random.normal(stream_key, shape, jnp.float32)
    if cuts:
        drawn = drawn * block_levels(stream_key, shape, cuts, -0.22, 0.18)
    return jnp.clip(raised(drawn, jax.random.fold_in(stream_key, 3), *heavy), -limit, limit).astype(kind)


def setup_inputs(seed: int = 0) -> dict:
    keys = jax.random.split(jax.random.key(seed), 4)
    return {
        "saved_input": noise(keys[0], (TOKENS, H), 1.0, 6.0, ((0, 8), (1, 32))),
        "out_grad": gaussian_with(keys[1], (TOKENS, D), (TOKENS // 4) ** -0.5, 0.75, ((0, 32), (1, 8)), (1, 0, 32, 2.75)),
        "weight": noise(keys[2], (H, D), (D // 128) ** -0.5, 0.625, ((0, 32), (1, 8))),
    }


def gelu_parts(values):
    coeff = math.sqrt(2.0 / math.pi)
    inner = jnp.tanh(coeff * (values + 0.044715 * values * values * values))
    gelu_value = 0.5 * values * (1.0 + inner)
    gelu_slope = 0.5 * (1.0 + inner) + 0.5 * values * (1.0 - inner * inner) * coeff * (1.0 + 3.0 * 0.044715 * values * values)
    return (gelu_value, gelu_slope)

def reference(saved_input, out_grad, weight):
    values = saved_input.astype(jnp.float32)
    gelu_value, gelu_slope = gelu_parts(values)
    hidden = gelu_value.astype(jnp.bfloat16)
    back = lax.dot_general(out_grad, weight, (((1,), (1,)), ((), ())), preferred_element_type=jnp.float32)
    in_grad = (back * gelu_slope).astype(jnp.bfloat16)
    weight_grad = lax.dot_general(hidden, out_grad, (((0,), (0,)), ((), ())), preferred_element_type=jnp.float32)
    return (in_grad, weight_grad.astype(jnp.bfloat16))
```

```python
import math

import jax
import jax.numpy as jnp
from jax import lax
from jax.sharding import PartitionSpec as P


def gelu_parts(values):
    coeff = math.sqrt(2.0 / math.pi)
    inner = jnp.tanh(coeff * (values + 0.044715 * values * values * values))
    gelu_value = 0.5 * values * (1.0 + inner)
    gelu_slope = 0.5 * (1.0 + inner) + 0.5 * values * (1.0 - inner * inner) * coeff * (
        1.0 + 3.0 * 0.044715 * values * values
    )
    return (gelu_value, gelu_slope)


def chip_shift(n_col, s):
    n_x = n_col // 2
    return [(x * 2 + k, ((x + s) % n_x) * 2 + k) for x in range(n_x) for k in range(2)]


def core_swap(n_col):
    return [(c, c ^ 1) for c in range(n_col)]


def make_per_device(n_col):
    n_x = n_col // 2

    def per_device(saved_input, out_grad, weight):
        c = lax.axis_index("col")
        x = c // 2
        k = c % 2

        grad_all = lax.all_gather(out_grad, "row", axis=0, tiled=True)

        got = [saved_input]
        for s in range(1, n_x):
            got.append(lax.ppermute(saved_input, "col", chip_shift(n_col, s)))
        by_chip = jnp.stack(got, axis=0)
        order = (x - jnp.arange(n_x)) % n_x
        mine_by_x = jnp.take(by_chip, order, axis=0)
        other_by_x = lax.ppermute(mine_by_x, "col", core_swap(n_col))
        pair = jnp.where(k == 0, jnp.stack([mine_by_x, other_by_x], axis=1),
                         jnp.stack([other_by_x, mine_by_x], axis=1))
        saved_all = pair.reshape((n_col * saved_input.shape[0], saved_input.shape[1]))

        gelu_value, unused_slope = gelu_parts(saved_all.astype(jnp.float32))
        hidden = gelu_value.astype(jnp.bfloat16)
        weight_grad = lax.dot_general(
            hidden, grad_all, (((0,), (0,)), ((), ())), preferred_element_type=jnp.float32
        ).astype(jnp.bfloat16)

        partial = lax.dot_general(
            grad_all, weight, (((1,), (1,)), ((), ())), preferred_element_type=jnp.float32
        )
        rows = saved_input.shape[0]
        p4 = partial.reshape((n_x, 2, rows, partial.shape[1]))
        mine = lax.dynamic_index_in_dim(p4, k, axis=1, keepdims=False)
        theirs = lax.dynamic_index_in_dim(p4, 1 - k, axis=1, keepdims=False)
        chip_sum = mine + lax.ppermute(theirs, "col", core_swap(n_col))
        back = lax.dynamic_index_in_dim(chip_sum, x, axis=0, keepdims=False)
        for s in range(1, n_x):
            dest = lax.dynamic_index_in_dim(chip_sum, (x + s) % n_x, axis=0, keepdims=False)
            recv = lax.ppermute(dest.astype(jnp.bfloat16), "col", chip_shift(n_col, s))
            back = back + recv.astype(jnp.float32)

        unused_value, own_slope = gelu_parts(saved_input.astype(jnp.float32))
        in_grad = (back * own_slope).astype(jnp.bfloat16)
        return (in_grad, weight_grad)

    return per_device


def solution(mesh):
    in_specs = (P("col", "row"), P("row", "col"), P("row", "col"))
    out_specs = (P("col", "row"), P("row", "col"))
    return jax.shard_map(
        make_per_device(mesh.shape["col"]),
        mesh=mesh, in_specs=in_specs, out_specs=out_specs, check_vma=False,
    )
```

```python
import math

import jax
import jax.numpy as jnp
from jax import lax
from jax.sharding import Mesh, PartitionSpec as P

COL = ("x", "c")


def gelu_parts(values):
    coeff = math.sqrt(2.0 / math.pi)
    inner = jnp.tanh(coeff * (values + 0.044715 * values * values * values))
    gelu_value = 0.5 * values * (1.0 + inner)
    gelu_slope = 0.5 * (1.0 + inner) + 0.5 * values * (1.0 - inner * inner) * coeff * (
        1.0 + 3.0 * 0.044715 * values * values
    )
    return (gelu_value, gelu_slope)


def chip_shift(n_col, s):
    n_x = n_col // 2
    return [(x * 2 + k, ((x + s) % n_x) * 2 + k) for x in range(n_x) for k in range(2)]


def core_swap(n_col):
    return [(c, c ^ 1) for c in range(n_col)]


def make_per_device(n_col):
    n_x = n_col // 2

    def per_device(saved_input, out_grad, weight):
        c = lax.axis_index(COL)
        x = c // 2
        k = c % 2

        grad_y = lax.all_gather(out_grad, "y", axis=0, tiled=True)
        grad_all = lax.all_gather(grad_y, "z", axis=0, tiled=True)

        got = [saved_input]
        for s in range(1, n_x):
            got.append(lax.ppermute(saved_input, COL, chip_shift(n_col, s)))
        by_chip = jnp.stack(got, axis=0)
        order = (x - jnp.arange(n_x)) % n_x
        mine_by_x = jnp.take(by_chip, order, axis=0)
        other_by_x = lax.ppermute(mine_by_x, COL, core_swap(n_col))
        pair = jnp.where(k == 0, jnp.stack([mine_by_x, other_by_x], axis=1),
                         jnp.stack([other_by_x, mine_by_x], axis=1))
        saved_all = pair.reshape((n_col * saved_input.shape[0], saved_input.shape[1]))

        gelu_value, unused_slope = gelu_parts(saved_all.astype(jnp.float32))
        hidden = gelu_value.astype(jnp.bfloat16)
        weight_grad = lax.dot_general(
            hidden, grad_all, (((0,), (0,)), ((), ())), preferred_element_type=jnp.float32
        ).astype(jnp.bfloat16)

        partial = lax.dot_general(
            grad_all, weight, (((1,), (1,)), ((), ())), preferred_element_type=jnp.float32
        )
        rows = saved_input.shape[0]
        p4 = partial.reshape((n_x, 2, rows, partial.shape[1]))
        mine = lax.dynamic_index_in_dim(p4, k, axis=1, keepdims=False)
        theirs = lax.dynamic_index_in_dim(p4, 1 - k, axis=1, keepdims=False)
        chip_sum = mine + lax.ppermute(theirs, COL, core_swap(n_col))
        back = lax.dynamic_index_in_dim(chip_sum, x, axis=0, keepdims=False)
        for s in range(1, n_x):
            dest = lax.dynamic_index_in_dim(chip_sum, (x + s) % n_x, axis=0, keepdims=False)
            recv = lax.ppermute(dest.astype(jnp.bfloat16), COL, chip_shift(n_col, s))
            back = back + recv.astype(jnp.float32)

        unused_value, own_slope = gelu_parts(saved_input.astype(jnp.float32))
        in_grad = (back * own_slope).astype(jnp.bfloat16)
        return (in_grad, weight_grad)

    return per_device


def solution(mesh):
    n_row, n_col = mesh.shape["row"], mesh.shape["col"]
    grid = Mesh(mesh.devices.reshape(n_row // 4, 4, n_col // 2, 2), ("z", "y", "x", "c"))
    row = ("z", "y")
    in_specs = (P(COL, row), P(row, COL), P(row, COL))
    out_specs = (P(COL, row), P(row, COL))
    return jax.shard_map(
        make_per_device(n_col),
        mesh=grid, in_specs=in_specs, out_specs=out_specs, check_vma=False,
    )
```

```python
import math

import jax
import jax.numpy as jnp
from jax import lax
from jax.sharding import Mesh, PartitionSpec as P

COL = ("x", "c")


def gelu_parts(values):
    coeff = math.sqrt(2.0 / math.pi)
    inner = jnp.tanh(coeff * (values + 0.044715 * values * values * values))
    gelu_value = 0.5 * values * (1.0 + inner)
    gelu_slope = 0.5 * (1.0 + inner) + 0.5 * values * (1.0 - inner * inner) * coeff * (
        1.0 + 3.0 * 0.044715 * values * values
    )
    return (gelu_value, gelu_slope)


def chip_shift(n_col, s):
    n_x = n_col // 2
    return [(x * 2 + k, ((x + s) % n_x) * 2 + k) for x in range(n_x) for k in range(2)]


def core_swap(n_col):
    return [(c, c ^ 1) for c in range(n_col)]


def ring_gather(block, axis, n):
    i = lax.axis_index(axis)
    fwd = bwd = block
    by_off = {0: block}
    for step in range(1, n // 2 + 1):
        ahead = [(j, (j + 1) % n) for j in range(n)]
        behind = [(j, (j - 1) % n) for j in range(n)]
        if 2 * step == n:
            half = block.shape[-1] // 2
            from_behind = lax.ppermute(fwd[..., :half], axis, ahead)
            from_ahead = lax.ppermute(bwd[..., half:], axis, behind)
            by_off[step] = jnp.concatenate([from_behind, from_ahead], axis=-1)
        else:
            fwd = lax.ppermute(fwd, axis, ahead)
            bwd = lax.ppermute(bwd, axis, behind)
            by_off[-step % n] = fwd
            by_off[step] = bwd
    stacked = jnp.stack([by_off[d] for d in range(n)], axis=0)
    return jnp.roll(stacked, i, axis=0)


def make_per_device(n_col, n_z, n_y):
    n_x = n_col // 2

    def per_device(saved_input, out_grad, weight):
        c = lax.axis_index(COL)
        x = c // 2
        k = c % 2

        tokens = out_grad.shape[0] * n_z * n_y
        half = out_grad.shape[1] // 2
        part_a = ring_gather(ring_gather(out_grad[:, :half], "z", n_z), "y", n_y)
        part_b = ring_gather(ring_gather(out_grad[:, half:], "y", n_y), "z", n_z)
        part_a = jnp.swapaxes(part_a, 0, 1).reshape((tokens, half))
        part_b = part_b.reshape((tokens, out_grad.shape[1] - half))
        grad_all = jnp.concatenate([part_a, part_b], axis=1)

        got = [saved_input]
        for s in range(1, n_x):
            got.append(lax.ppermute(saved_input, COL, chip_shift(n_col, s)))
        by_chip = jnp.stack(got, axis=0)
        order = (x - jnp.arange(n_x)) % n_x
        mine_by_x = jnp.take(by_chip, order, axis=0)
        other_by_x = lax.ppermute(mine_by_x, COL, core_swap(n_col))
        pair = jnp.where(k == 0, jnp.stack([mine_by_x, other_by_x], axis=1),
                         jnp.stack([other_by_x, mine_by_x], axis=1))
        saved_all = pair.reshape((n_col * saved_input.shape[0], saved_input.shape[1]))

        gelu_value, unused_slope = gelu_parts(saved_all.astype(jnp.float32))
        hidden = gelu_value.astype(jnp.bfloat16)
        weight_grad = lax.dot_general(
            hidden, grad_all, (((0,), (0,)), ((), ())), preferred_element_type=jnp.float32
        ).astype(jnp.bfloat16)

        partial = lax.dot_general(
            grad_all, weight, (((1,), (1,)), ((), ())), preferred_element_type=jnp.float32
        )
        rows = saved_input.shape[0]
        p4 = partial.reshape((n_x, 2, rows, partial.shape[1]))
        mine = lax.dynamic_index_in_dim(p4, k, axis=1, keepdims=False)
        theirs = lax.dynamic_index_in_dim(p4, 1 - k, axis=1, keepdims=False)
        chip_sum = mine + lax.ppermute(theirs, COL, core_swap(n_col))
        back = lax.dynamic_index_in_dim(chip_sum, x, axis=0, keepdims=False)
        for s in range(1, n_x):
            dest = lax.dynamic_index_in_dim(chip_sum, (x + s) % n_x, axis=0, keepdims=False)
            recv = lax.ppermute(dest.astype(jnp.bfloat16), COL, chip_shift(n_col, s))
            back = back + recv.astype(jnp.float32)

        unused_value, own_slope = gelu_parts(saved_input.astype(jnp.float32))
        in_grad = (back * own_slope).astype(jnp.bfloat16)
        return (in_grad, weight_grad)

    return per_device


def solution(mesh):
    n_row, n_col = mesh.shape["row"], mesh.shape["col"]
    grid = Mesh(mesh.devices.reshape(n_row // 4, 4, n_col // 2, 2), ("z", "y", "x", "c"))
    row = ("z", "y")
    in_specs = (P(COL, row), P(row, COL), P(row, COL))
    out_specs = (P(COL, row), P(row, COL))
    return jax.shard_map(
        make_per_device(n_col, n_row // 4, 4),
        mesh=grid, in_specs=in_specs, out_specs=out_specs, check_vma=False,
    )
```

```python
import math

import jax
import jax.numpy as jnp
from jax import lax
from jax.sharding import Mesh, PartitionSpec as P

COL = ("x", "c")


def gelu_parts(values):
    coeff = math.sqrt(2.0 / math.pi)
    inner = jnp.tanh(coeff * (values + 0.044715 * values * values * values))
    gelu_value = 0.5 * values * (1.0 + inner)
    gelu_slope = 0.5 * (1.0 + inner) + 0.5 * values * (1.0 - inner * inner) * coeff * (
        1.0 + 3.0 * 0.044715 * values * values
    )
    return (gelu_value, gelu_slope)


def chip_shift(n_col, s):
    n_x = n_col // 2
    return [(x * 2 + k, ((x + s) % n_x) * 2 + k) for x in range(n_x) for k in range(2)]


def core_swap(n_col):
    return [(c, c ^ 1) for c in range(n_col)]


def ring_gather(block, axis, n):
    i = lax.axis_index(axis)
    fwd = bwd = block
    by_off = {0: block}
    for step in range(1, n // 2 + 1):
        ahead = [(j, (j + 1) % n) for j in range(n)]
        behind = [(j, (j - 1) % n) for j in range(n)]
        if 2 * step == n:
            half = block.shape[-1] // 2
            from_behind = lax.ppermute(fwd[..., :half], axis, ahead)
            from_ahead = lax.ppermute(bwd[..., half:], axis, behind)
            by_off[step] = jnp.concatenate([from_behind, from_ahead], axis=-1)
        else:
            fwd = lax.ppermute(fwd, axis, ahead)
            bwd = lax.ppermute(bwd, axis, behind)
            by_off[-step % n] = fwd
            by_off[step] = bwd
    stacked = jnp.stack([by_off[d] for d in range(n)], axis=0)
    return jnp.roll(stacked, i, axis=0)


def make_per_device(n_col, n_z, n_y):
    n_x = n_col // 2

    def per_device(saved_input, out_grad, weight):
        c = lax.axis_index(COL)
        x = c // 2
        k = c % 2

        tokens = out_grad.shape[0] * n_z * n_y
        half = out_grad.shape[1] // 2
        gather_z = lambda a: lax.all_gather(a, "z", axis=0, tiled=False)
        part_a = ring_gather(gather_z(out_grad[:, :half]), "y", n_y)
        part_b = gather_z(ring_gather(out_grad[:, half:], "y", n_y))
        part_a = jnp.swapaxes(part_a, 0, 1).reshape((tokens, half))
        part_b = part_b.reshape((tokens, out_grad.shape[1] - half))
        grad_all = jnp.concatenate([part_a, part_b], axis=1)

        got = [saved_input]
        for s in range(1, n_x):
            got.append(lax.ppermute(saved_input, COL, chip_shift(n_col, s)))
        by_chip = jnp.stack(got, axis=0)
        order = (x - jnp.arange(n_x)) % n_x
        mine_by_x = jnp.take(by_chip, order, axis=0)
        other_by_x = lax.ppermute(mine_by_x, COL, core_swap(n_col))
        pair = jnp.where(k == 0, jnp.stack([mine_by_x, other_by_x], axis=1),
                         jnp.stack([other_by_x, mine_by_x], axis=1))
        saved_all = pair.reshape((n_col * saved_input.shape[0], saved_input.shape[1]))

        gelu_value, unused_slope = gelu_parts(saved_all.astype(jnp.float32))
        hidden = gelu_value.astype(jnp.bfloat16)
        weight_grad = lax.dot_general(
            hidden, grad_all, (((0,), (0,)), ((), ())), preferred_element_type=jnp.float32
        ).astype(jnp.bfloat16)

        partial = lax.dot_general(
            grad_all, weight, (((1,), (1,)), ((), ())), preferred_element_type=jnp.float32
        )
        rows = saved_input.shape[0]
        p4 = partial.reshape((n_x, 2, rows, partial.shape[1]))
        mine = lax.dynamic_index_in_dim(p4, k, axis=1, keepdims=False)
        theirs = lax.dynamic_index_in_dim(p4, 1 - k, axis=1, keepdims=False)
        chip_sum = mine + lax.ppermute(theirs, COL, core_swap(n_col))
        back = lax.dynamic_index_in_dim(chip_sum, x, axis=0, keepdims=False)
        for s in range(1, n_x):
            dest = lax.dynamic_index_in_dim(chip_sum, (x + s) % n_x, axis=0, keepdims=False)
            recv = lax.ppermute(dest.astype(jnp.bfloat16), COL, chip_shift(n_col, s))
            back = back + recv.astype(jnp.float32)

        unused_value, own_slope = gelu_parts(saved_input.astype(jnp.float32))
        in_grad = (back * own_slope).astype(jnp.bfloat16)
        return (in_grad, weight_grad)

    return per_device


def solution(mesh):
    n_row, n_col = mesh.shape["row"], mesh.shape["col"]
    grid = Mesh(mesh.devices.reshape(n_row // 4, 4, n_col // 2, 2), ("z", "y", "x", "c"))
    row = ("z", "y")
    in_specs = (P(COL, row), P(row, COL), P(row, COL))
    out_specs = (P(COL, row), P(row, COL))
    return jax.shard_map(
        make_per_device(n_col, n_row // 4, 4),
        mesh=grid, in_specs=in_specs, out_specs=out_specs, check_vma=False,
    )
```

```python
import math

import jax
import jax.numpy as jnp
from jax import lax
from jax.sharding import Mesh, PartitionSpec as P

COL = ("x", "c")


def gelu_parts(values):
    coeff = math.sqrt(2.0 / math.pi)
    inner = jnp.tanh(coeff * (values + 0.044715 * values * values * values))
    gelu_value = 0.5 * values * (1.0 + inner)
    gelu_slope = 0.5 * (1.0 + inner) + 0.5 * values * (1.0 - inner * inner) * coeff * (
        1.0 + 3.0 * 0.044715 * values * values
    )
    return (gelu_value, gelu_slope)


def chip_shift(n_col, s):
    n_x = n_col // 2
    return [(x * 2 + k, ((x + s) % n_x) * 2 + k) for x in range(n_x) for k in range(2)]


def core_swap(n_col):
    return [(c, c ^ 1) for c in range(n_col)]


def ring_gather(block, axis, n):
    i = lax.axis_index(axis)
    fwd = bwd = block
    by_off = {0: block}
    for step in range(1, n // 2 + 1):
        ahead = [(j, (j + 1) % n) for j in range(n)]
        behind = [(j, (j - 1) % n) for j in range(n)]
        if 2 * step == n:
            half = block.shape[-1] // 2
            from_behind = lax.ppermute(fwd[..., :half], axis, ahead)
            from_ahead = lax.ppermute(bwd[..., half:], axis, behind)
            by_off[step] = jnp.concatenate([from_behind, from_ahead], axis=-1)
        else:
            fwd = lax.ppermute(fwd, axis, ahead)
            bwd = lax.ppermute(bwd, axis, behind)
            by_off[-step % n] = fwd
            by_off[step] = bwd
    stacked = jnp.stack([by_off[d] for d in range(n)], axis=0)
    return jnp.roll(stacked, i, axis=0)


def make_per_device(n_col, n_z, n_y):
    n_x = n_col // 2

    def per_device(saved_input, out_grad, weight):
        c = lax.axis_index(COL)
        x = c // 2
        k = c % 2

        tokens = out_grad.shape[0] * n_z * n_y
        half = out_grad.shape[1] // 2
        part_a = ring_gather(ring_gather(out_grad[:, :half], "z", n_z), "y", n_y)
        part_b = lax.all_gather(ring_gather(out_grad[:, half:], "y", n_y), "z", axis=0)
        part_a = jnp.swapaxes(part_a, 0, 1).reshape((tokens, half))
        part_b = part_b.reshape((tokens, out_grad.shape[1] - half))
        grad_all = jnp.concatenate([part_a, part_b], axis=1)

        saved_after, part_b = lax.optimization_barrier((saved_input, part_b))
        saved_all = lax.all_gather(saved_after, COL, axis=0, tiled=True)

        gelu_value, unused_slope = gelu_parts(saved_all.astype(jnp.float32))
        hidden = gelu_value.astype(jnp.bfloat16)
        weight_grad = lax.dot_general(
            hidden, grad_all, (((0,), (0,)), ((), ())), preferred_element_type=jnp.float32
        ).astype(jnp.bfloat16)

        partial = lax.dot_general(
            grad_all, weight, (((1,), (1,)), ((), ())), preferred_element_type=jnp.float32
        )
        rows = saved_input.shape[0]
        p4 = partial.reshape((n_x, 2, rows, partial.shape[1]))
        mine = lax.dynamic_index_in_dim(p4, k, axis=1, keepdims=False)
        theirs = lax.dynamic_index_in_dim(p4, 1 - k, axis=1, keepdims=False)
        chip_sum = mine + lax.ppermute(theirs, COL, core_swap(n_col))
        back = lax.dynamic_index_in_dim(chip_sum, x, axis=0, keepdims=False)
        for s in range(1, n_x):
            dest = lax.dynamic_index_in_dim(chip_sum, (x + s) % n_x, axis=0, keepdims=False)
            recv = lax.ppermute(dest.astype(jnp.bfloat16), COL, chip_shift(n_col, s))
            back = back + recv.astype(jnp.float32)

        unused_value, own_slope = gelu_parts(saved_input.astype(jnp.float32))
        in_grad = (back * own_slope).astype(jnp.bfloat16)
        return (in_grad, weight_grad)

    return per_device


def solution(mesh):
    n_row, n_col = mesh.shape["row"], mesh.shape["col"]
    grid = Mesh(mesh.devices.reshape(n_row // 4, 4, n_col // 2, 2), ("z", "y", "x", "c"))
    row = ("z", "y")
    in_specs = (P(COL, row), P(row, COL), P(row, COL))
    out_specs = (P(COL, row), P(row, COL))
    return jax.shard_map(
        make_per_device(n_col, n_row // 4, 4),
        mesh=grid, in_specs=in_specs, out_specs=out_specs, check_vma=False,
    )
```

```python
import math

import jax
import jax.numpy as jnp
from jax import lax
from jax.sharding import Mesh, PartitionSpec as P

COL = ("x", "c")


def gelu_parts(values):
    coeff = math.sqrt(2.0 / math.pi)
    inner = jnp.tanh(coeff * (values + 0.044715 * values * values * values))
    gelu_value = 0.5 * values * (1.0 + inner)
    gelu_slope = 0.5 * (1.0 + inner) + 0.5 * values * (1.0 - inner * inner) * coeff * (
        1.0 + 3.0 * 0.044715 * values * values
    )
    return (gelu_value, gelu_slope)


def chip_shift(n_col, s):
    n_x = n_col // 2
    return [(x * 2 + k, ((x + s) % n_x) * 2 + k) for x in range(n_x) for k in range(2)]


def core_swap(n_col):
    return [(c, c ^ 1) for c in range(n_col)]


def ring_gather(block, axis, n):
    i = lax.axis_index(axis)
    fwd = bwd = block
    by_off = {0: block}
    for step in range(1, n // 2 + 1):
        ahead = [(j, (j + 1) % n) for j in range(n)]
        behind = [(j, (j - 1) % n) for j in range(n)]
        if 2 * step == n:
            half = block.shape[-1] // 2
            from_behind = lax.ppermute(fwd[..., :half], axis, ahead)
            from_ahead = lax.ppermute(bwd[..., half:], axis, behind)
            by_off[step] = jnp.concatenate([from_behind, from_ahead], axis=-1)
        else:
            fwd = lax.ppermute(fwd, axis, ahead)
            bwd = lax.ppermute(bwd, axis, behind)
            by_off[-step % n] = fwd
            by_off[step] = bwd
    stacked = jnp.stack([by_off[d] for d in range(n)], axis=0)
    return jnp.roll(stacked, i, axis=0)


def make_per_device(n_col, n_z, n_y):
    n_x = n_col // 2

    def per_device(saved_input, out_grad, weight):
        c = lax.axis_index(COL)
        x = c // 2
        k = c % 2

        tokens = out_grad.shape[0] * n_z * n_y
        gathered = ring_gather(ring_gather(out_grad, "z", n_z), "y", n_y)
        grad_all = jnp.swapaxes(gathered, 0, 1).reshape((tokens, out_grad.shape[1]))

        got = [saved_input]
        for s in range(1, n_x):
            got.append(lax.ppermute(saved_input, COL, chip_shift(n_col, s)))
        by_chip = jnp.stack(got, axis=0)
        order = (x - jnp.arange(n_x)) % n_x
        mine_by_x = jnp.take(by_chip, order, axis=0)
        other_by_x = lax.ppermute(mine_by_x, COL, core_swap(n_col))
        pair = jnp.where(k == 0, jnp.stack([mine_by_x, other_by_x], axis=1),
                         jnp.stack([other_by_x, mine_by_x], axis=1))
        saved_all = pair.reshape((n_col * saved_input.shape[0], saved_input.shape[1]))

        gelu_value, unused_slope = gelu_parts(saved_all.astype(jnp.float32))
        hidden = gelu_value.astype(jnp.bfloat16)
        weight_grad = lax.dot_general(
            hidden, grad_all, (((0,), (0,)), ((), ())), preferred_element_type=jnp.float32
        ).astype(jnp.bfloat16)

        partial = lax.dot_general(
            grad_all, weight, (((1,), (1,)), ((), ())), preferred_element_type=jnp.float32
        )
        rows = saved_input.shape[0]
        p4 = partial.reshape((n_x, 2, rows, partial.shape[1]))
        mine = lax.dynamic_index_in_dim(p4, k, axis=1, keepdims=False)
        theirs = lax.dynamic_index_in_dim(p4, 1 - k, axis=1, keepdims=False)
        chip_sum = mine + lax.ppermute(theirs, COL, core_swap(n_col))
        back = lax.dynamic_index_in_dim(chip_sum, x, axis=0, keepdims=False)
        for s in range(1, n_x):
            dest = lax.dynamic_index_in_dim(chip_sum, (x + s) % n_x, axis=0, keepdims=False)
            recv = lax.ppermute(dest.astype(jnp.bfloat16), COL, chip_shift(n_col, s))
            back = back + recv.astype(jnp.float32)

        unused_value, own_slope = gelu_parts(saved_input.astype(jnp.float32))
        in_grad = (back * own_slope).astype(jnp.bfloat16)
        return (in_grad, weight_grad)

    return per_device


def solution(mesh):
    n_row, n_col = mesh.shape["row"], mesh.shape["col"]
    grid = Mesh(mesh.devices.reshape(n_row // 4, 4, n_col // 2, 2), ("z", "y", "x", "c"))
    row = ("z", "y")
    in_specs = (P(COL, row), P(row, COL), P(row, COL))
    out_specs = (P(COL, row), P(row, COL))
    return jax.shard_map(
        make_per_device(n_col, n_row // 4, 4),
        mesh=grid, in_specs=in_specs, out_specs=out_specs, check_vma=False,
    )
```

```python
import math

import jax
import jax.numpy as jnp
from jax import lax
from jax.sharding import Mesh, PartitionSpec as P

COL = ("x", "c")


def gelu_parts(values):
    coeff = math.sqrt(2.0 / math.pi)
    inner = jnp.tanh(coeff * (values + 0.044715 * values * values * values))
    gelu_value = 0.5 * values * (1.0 + inner)
    gelu_slope = 0.5 * (1.0 + inner) + 0.5 * values * (1.0 - inner * inner) * coeff * (
        1.0 + 3.0 * 0.044715 * values * values
    )
    return (gelu_value, gelu_slope)


def chip_shift(n_col, s):
    n_x = n_col // 2
    return [(x * 2 + k, ((x + s) % n_x) * 2 + k) for x in range(n_x) for k in range(2)]


def core_swap(n_col):
    return [(c, c ^ 1) for c in range(n_col)]


def ring_gather(block, axis, n):
    i = lax.axis_index(axis)
    fwd = bwd = block
    by_off = {0: block}
    for step in range(1, n // 2 + 1):
        ahead = [(j, (j + 1) % n) for j in range(n)]
        behind = [(j, (j - 1) % n) for j in range(n)]
        if 2 * step == n:
            half = block.shape[-1] // 2
            from_behind = lax.ppermute(fwd[..., :half], axis, ahead)
            from_ahead = lax.ppermute(bwd[..., half:], axis, behind)
            by_off[step] = jnp.concatenate([from_behind, from_ahead], axis=-1)
        else:
            fwd = lax.ppermute(fwd, axis, ahead)
            bwd = lax.ppermute(bwd, axis, behind)
            by_off[-step % n] = fwd
            by_off[step] = bwd
    stacked = jnp.stack([by_off[d] for d in range(n)], axis=0)
    return jnp.roll(stacked, i, axis=0)


def make_per_device(n_col, n_z, n_y):
    n_x = n_col // 2

    def per_device(saved_input, out_grad, weight):
        c = lax.axis_index(COL)
        x = c // 2
        k = c % 2

        tokens = out_grad.shape[0] * n_z * n_y
        gathered = ring_gather(ring_gather(out_grad, "z", n_z), "y", n_y)
        grad_all = gathered.reshape((tokens, out_grad.shape[1]))
        rows_r = out_grad.shape[0]

        got = [saved_input]
        for s in range(1, n_x):
            got.append(lax.ppermute(saved_input, COL, chip_shift(n_col, s)))
        by_chip = jnp.stack(got, axis=0)
        order = (x - jnp.arange(n_x)) % n_x
        mine_by_x = jnp.take(by_chip, order, axis=0)
        other_by_x = lax.ppermute(mine_by_x, COL, core_swap(n_col))
        pair = jnp.where(k == 0, jnp.stack([mine_by_x, other_by_x], axis=1),
                         jnp.stack([other_by_x, mine_by_x], axis=1))
        saved_all = pair.reshape((n_col * saved_input.shape[0], saved_input.shape[1]))

        gelu_value, unused_slope = gelu_parts(saved_all.astype(jnp.float32))
        hidden = gelu_value.astype(jnp.bfloat16).reshape((n_z, n_y, rows_r, -1))
        hidden = jnp.swapaxes(hidden, 0, 1).reshape((tokens, -1))
        weight_grad = lax.dot_general(
            hidden, grad_all, (((0,), (0,)), ((), ())), preferred_element_type=jnp.float32
        ).astype(jnp.bfloat16)

        partial = lax.dot_general(
            grad_all, weight, (((1,), (1,)), ((), ())), preferred_element_type=jnp.float32
        )
        rows = saved_input.shape[0]
        p_nat = jnp.swapaxes(partial.reshape((n_y, n_z, rows_r, -1)), 0, 1)
        p4 = p_nat.reshape((n_x, 2, rows, partial.shape[1]))
        mine = lax.dynamic_index_in_dim(p4, k, axis=1, keepdims=False)
        theirs = lax.dynamic_index_in_dim(p4, 1 - k, axis=1, keepdims=False)
        chip_sum = mine + lax.ppermute(theirs, COL, core_swap(n_col))
        back = lax.dynamic_index_in_dim(chip_sum, x, axis=0, keepdims=False)
        dest = lambda s: lax.dynamic_index_in_dim(
            chip_sum, (x + s) % n_x, axis=0, keepdims=False).astype(jnp.bfloat16)
        if n_x == 4:
            cut = chip_sum.shape[-1] // 2
            far = dest(2)
            up, up_relay = lax.ppermute((dest(1), far[:, :cut]), COL, chip_shift(n_col, 1))
            dn, dn_relay = lax.ppermute((dest(-1), far[:, cut:]), COL, chip_shift(n_col, -1))
            far_lo = lax.ppermute(up_relay, COL, chip_shift(n_col, 1))
            far_hi = lax.ppermute(dn_relay, COL, chip_shift(n_col, -1))
            far_got = jnp.concatenate([far_lo, far_hi], axis=-1)
            for recv in (up, dn, far_got):
                back = back + recv.astype(jnp.float32)
        else:
            for s in range(1, n_x):
                recv = lax.ppermute(dest(s), COL, chip_shift(n_col, s))
                back = back + recv.astype(jnp.float32)

        unused_value, own_slope = gelu_parts(saved_input.astype(jnp.float32))
        in_grad = (back * own_slope).astype(jnp.bfloat16)
        return (in_grad, weight_grad)

    return per_device


def solution(mesh):
    n_row, n_col = mesh.shape["row"], mesh.shape["col"]
    grid = Mesh(mesh.devices.reshape(n_row // 4, 4, n_col // 2, 2), ("z", "y", "x", "c"))
    row = ("z", "y")
    in_specs = (P(COL, row), P(row, COL), P(row, COL))
    out_specs = (P(COL, row), P(row, COL))
    return jax.shard_map(
        make_per_device(n_col, n_row // 4, 4),
        mesh=grid, in_specs=in_specs, out_specs=out_specs, check_vma=False,
    )
```

```python
import math

import jax
import jax.numpy as jnp
from jax import lax
from jax.sharding import Mesh, PartitionSpec as P

COL = ("x", "c")


def gelu_parts(values):
    coeff = math.sqrt(2.0 / math.pi)
    inner = jnp.tanh(coeff * (values + 0.044715 * values * values * values))
    gelu_value = 0.5 * values * (1.0 + inner)
    gelu_slope = 0.5 * (1.0 + inner) + 0.5 * values * (1.0 - inner * inner) * coeff * (
        1.0 + 3.0 * 0.044715 * values * values
    )
    return (gelu_value, gelu_slope)


def chip_shift(n_col, s):
    n_x = n_col // 2
    return [(x * 2 + k, ((x + s) % n_x) * 2 + k) for x in range(n_x) for k in range(2)]


def core_swap(n_col):
    return [(c, c ^ 1) for c in range(n_col)]


def ring_gather(block, axis, n):
    i = lax.axis_index(axis)
    fwd = bwd = block
    by_off = {0: block}
    for step in range(1, n // 2 + 1):
        ahead = [(j, (j + 1) % n) for j in range(n)]
        behind = [(j, (j - 1) % n) for j in range(n)]
        if 2 * step == n:
            half = block.shape[-1] // 2
            from_behind = lax.ppermute(fwd[..., :half], axis, ahead)
            from_ahead = lax.ppermute(bwd[..., half:], axis, behind)
            by_off[step] = jnp.concatenate([from_behind, from_ahead], axis=-1)
        else:
            fwd = lax.ppermute(fwd, axis, ahead)
            bwd = lax.ppermute(bwd, axis, behind)
            by_off[-step % n] = fwd
            by_off[step] = bwd
    stacked = jnp.stack([by_off[d] for d in range(n)], axis=0)
    return jnp.roll(stacked, i, axis=0)


def make_per_device(n_col, n_z, n_y):
    n_x = n_col // 2

    def per_device(saved_input, out_grad, weight):
        c = lax.axis_index(COL)
        x = c // 2
        k = c % 2

        tokens = out_grad.shape[0] * n_z * n_y
        gathered = ring_gather(ring_gather(out_grad, "z", n_z), "y", n_y)
        grad_all = gathered.reshape((tokens, out_grad.shape[1]))
        rows_r = out_grad.shape[0]

        got = [saved_input]
        for s in range(1, n_x):
            got.append(lax.ppermute(saved_input, COL, chip_shift(n_col, s)))
        by_chip = jnp.stack(got, axis=0)
        order = (x - jnp.arange(n_x)) % n_x
        mine_by_x = jnp.take(by_chip, order, axis=0)
        other_by_x = lax.ppermute(mine_by_x, COL, core_swap(n_col))
        pair = jnp.where(k == 0, jnp.stack([mine_by_x, other_by_x], axis=1),
                         jnp.stack([other_by_x, mine_by_x], axis=1))
        saved_all = pair.reshape((n_col * saved_input.shape[0], saved_input.shape[1]))

        saved_all, grad_all = lax.optimization_barrier((saved_all, grad_all))
        gelu_value, unused_slope = gelu_parts(saved_all.astype(jnp.float32))
        hidden = gelu_value.astype(jnp.bfloat16).reshape((n_z, n_y, rows_r, -1))
        hidden = jnp.swapaxes(hidden, 0, 1).reshape((tokens, -1))
        weight_grad = lax.dot_general(
            hidden, grad_all, (((0,), (0,)), ((), ())), preferred_element_type=jnp.float32
        ).astype(jnp.bfloat16)

        partial = lax.dot_general(
            grad_all, weight, (((1,), (1,)), ((), ())), preferred_element_type=jnp.float32
        )
        rows = saved_input.shape[0]
        p_nat = jnp.swapaxes(partial.reshape((n_y, n_z, rows_r, -1)), 0, 1)
        p4 = p_nat.reshape((n_x, 2, rows, partial.shape[1]))
        mine = lax.dynamic_index_in_dim(p4, k, axis=1, keepdims=False)
        theirs = lax.dynamic_index_in_dim(p4, 1 - k, axis=1, keepdims=False)
        chip_sum = mine + lax.ppermute(theirs, COL, core_swap(n_col))
        back = lax.dynamic_index_in_dim(chip_sum, x, axis=0, keepdims=False)
        dest = lambda s: lax.dynamic_index_in_dim(
            chip_sum, (x + s) % n_x, axis=0, keepdims=False).astype(jnp.bfloat16)
        if n_x == 4:
            cut = chip_sum.shape[-1] // 2
            far = dest(2)
            up, up_relay = lax.ppermute((dest(1), far[:, :cut]), COL, chip_shift(n_col, 1))
            dn, dn_relay = lax.ppermute((dest(-1), far[:, cut:]), COL, chip_shift(n_col, -1))
            far_lo = lax.ppermute(up_relay, COL, chip_shift(n_col, 1))
            far_hi = lax.ppermute(dn_relay, COL, chip_shift(n_col, -1))
            far_got = jnp.concatenate([far_lo, far_hi], axis=-1)
            for recv in (up, dn, far_got):
                back = back + recv.astype(jnp.float32)
        else:
            for s in range(1, n_x):
                recv = lax.ppermute(dest(s), COL, chip_shift(n_col, s))
                back = back + recv.astype(jnp.float32)

        unused_value, own_slope = gelu_parts(saved_input.astype(jnp.float32))
        in_grad = (back * own_slope).astype(jnp.bfloat16)
        return (in_grad, weight_grad)

    return per_device


def solution(mesh):
    n_row, n_col = mesh.shape["row"], mesh.shape["col"]
    grid = Mesh(mesh.devices.reshape(n_row // 4, 4, n_col // 2, 2), ("z", "y", "x", "c"))
    row = ("z", "y")
    in_specs = (P(COL, row), P(row, COL), P(row, COL))
    out_specs = (P(COL, row), P(row, COL))
    return jax.shard_map(
        make_per_device(n_col, n_row // 4, 4),
        mesh=grid, in_specs=in_specs, out_specs=out_specs, check_vma=False,
    )
```

```python
import math

import jax
import jax.numpy as jnp
from jax import lax
from jax.sharding import Mesh, PartitionSpec as P

COL = ("x", "c")


def gelu_parts(values):
    coeff = math.sqrt(2.0 / math.pi)
    inner = jnp.tanh(coeff * (values + 0.044715 * values * values * values))
    gelu_value = 0.5 * values * (1.0 + inner)
    gelu_slope = 0.5 * (1.0 + inner) + 0.5 * values * (1.0 - inner * inner) * coeff * (
        1.0 + 3.0 * 0.044715 * values * values
    )
    return (gelu_value, gelu_slope)


def chip_shift(n_col, s):
    n_x = n_col // 2
    return [(x * 2 + k, ((x + s) % n_x) * 2 + k) for x in range(n_x) for k in range(2)]


def core_swap(n_col):
    return [(c, c ^ 1) for c in range(n_col)]


def ring_gather(block, axis, n):
    i = lax.axis_index(axis)
    fwd = bwd = block
    by_off = {0: block}
    for step in range(1, n // 2 + 1):
        ahead = [(j, (j + 1) % n) for j in range(n)]
        behind = [(j, (j - 1) % n) for j in range(n)]
        if 2 * step == n:
            half = block.shape[-1] // 2
            from_behind = lax.ppermute(fwd[..., :half], axis, ahead)
            from_ahead = lax.ppermute(bwd[..., half:], axis, behind)
            by_off[step] = jnp.concatenate([from_behind, from_ahead], axis=-1)
        else:
            fwd = lax.ppermute(fwd, axis, ahead)
            bwd = lax.ppermute(bwd, axis, behind)
            by_off[-step % n] = fwd
            by_off[step] = bwd
    stacked = jnp.stack([by_off[d] for d in range(n)], axis=0)
    return jnp.roll(stacked, i, axis=0)


def make_per_device(n_col, n_z, n_y):
    n_x = n_col // 2

    def per_device(saved_input, out_grad, weight):
        c = lax.axis_index(COL)
        x = c // 2
        k = c % 2

        tokens = out_grad.shape[0] * n_z * n_y
        gathered = ring_gather(ring_gather(out_grad, "z", n_z), "y", n_y)
        grad_all = gathered.reshape((tokens, out_grad.shape[1]))
        rows_r = out_grad.shape[0]

        got = [saved_input]
        for s in range(1, n_x):
            got.append(lax.ppermute(saved_input, COL, chip_shift(n_col, s)))
        by_chip = jnp.stack(got, axis=0)
        order = (x - jnp.arange(n_x)) % n_x
        mine_by_x = jnp.take(by_chip, order, axis=0)
        other_by_x = lax.ppermute(mine_by_x, COL, core_swap(n_col))
        pair = jnp.where(k == 0, jnp.stack([mine_by_x, other_by_x], axis=1),
                         jnp.stack([other_by_x, mine_by_x], axis=1))
        saved_all = pair.reshape((n_col * saved_input.shape[0], saved_input.shape[1]))

        saved_all, grad_all = lax.optimization_barrier((saved_all, grad_all))
        gelu_value, unused_slope = gelu_parts(saved_all.astype(jnp.float32))
        hidden = gelu_value.astype(jnp.bfloat16).reshape((n_z, n_y, rows_r, -1))
        hidden = jnp.swapaxes(hidden, 0, 1).reshape((tokens, -1))
        weight_grad = lax.dot_general(
            hidden, grad_all, (((0,), (0,)), ((), ())), preferred_element_type=jnp.float32
        ).astype(jnp.bfloat16)

        rows = saved_input.shape[0]
        if n_z == n_col:
            g = grad_all.reshape((n_y, n_x, 2, rows_r, -1))
            g_theirs = lax.dynamic_index_in_dim(g, 1 - k, axis=2, keepdims=False)
            g_mine = lax.dynamic_index_in_dim(g, k, axis=2, keepdims=False)
            p_theirs = lax.dot_general(g_theirs, weight, (((3,), (1,)), ((), ())),
                                       preferred_element_type=jnp.float32)
            got_theirs = lax.ppermute(p_theirs.astype(jnp.bfloat16), COL, core_swap(n_col))
            p_mine = lax.dot_general(g_mine, weight, (((3,), (1,)), ((), ())),
                                     preferred_element_type=jnp.float32)
            chip_sum = p_mine + got_theirs.astype(jnp.float32)
            pick = lambda c: lax.dynamic_index_in_dim(
                chip_sum, c, axis=1, keepdims=False).reshape((rows, -1))
        else:
            partial = lax.dot_general(
                grad_all, weight, (((1,), (1,)), ((), ())), preferred_element_type=jnp.float32
            )
            p_nat = jnp.swapaxes(partial.reshape((n_y, n_z, rows_r, -1)), 0, 1)
            p4 = p_nat.reshape((n_x, 2, rows, partial.shape[1]))
            mine = lax.dynamic_index_in_dim(p4, k, axis=1, keepdims=False)
            theirs = lax.dynamic_index_in_dim(p4, 1 - k, axis=1, keepdims=False)
            chip_sum = mine + lax.ppermute(theirs, COL, core_swap(n_col))
            pick = lambda c: lax.dynamic_index_in_dim(chip_sum, c, axis=0, keepdims=False)
        back = pick(x)
        dest = lambda s: pick((x + s) % n_x).astype(jnp.bfloat16)
        if n_x == 4:
            cut = back.shape[-1] // 2
            far = dest(2)
            up, up_relay = lax.ppermute((dest(1), far[:, :cut]), COL, chip_shift(n_col, 1))
            dn, dn_relay = lax.ppermute((dest(-1), far[:, cut:]), COL, chip_shift(n_col, -1))
            far_lo = lax.ppermute(up_relay, COL, chip_shift(n_col, 1))
            far_hi = lax.ppermute(dn_relay, COL, chip_shift(n_col, -1))
            far_got = jnp.concatenate([far_lo, far_hi], axis=-1)
            for recv in (up, dn, far_got):
                back = back + recv.astype(jnp.float32)
        else:
            for s in range(1, n_x):
                recv = lax.ppermute(dest(s), COL, chip_shift(n_col, s))
                back = back + recv.astype(jnp.float32)

        unused_value, own_slope = gelu_parts(saved_input.astype(jnp.float32))
        in_grad = (back * own_slope).astype(jnp.bfloat16)
        return (in_grad, weight_grad)

    return per_device


def solution(mesh):
    n_row, n_col = mesh.shape["row"], mesh.shape["col"]
    grid = Mesh(mesh.devices.reshape(n_row // 4, 4, n_col // 2, 2), ("z", "y", "x", "c"))
    row = ("z", "y")
    in_specs = (P(COL, row), P(row, COL), P(row, COL))
    out_specs = (P(COL, row), P(row, COL))
    return jax.shard_map(
        make_per_device(n_col, n_row // 4, 4),
        mesh=grid, in_specs=in_specs, out_specs=out_specs, check_vma=False,
    )
```

```python
import math

import jax
import jax.numpy as jnp
from jax import lax
from jax.sharding import Mesh, PartitionSpec as P

COL = ("x", "c")


def gelu_parts(values):
    coeff = math.sqrt(2.0 / math.pi)
    inner = jnp.tanh(coeff * (values + 0.044715 * values * values * values))
    gelu_value = 0.5 * values * (1.0 + inner)
    gelu_slope = 0.5 * (1.0 + inner) + 0.5 * values * (1.0 - inner * inner) * coeff * (
        1.0 + 3.0 * 0.044715 * values * values
    )
    return (gelu_value, gelu_slope)


def chip_shift(n_col, s):
    n_x = n_col // 2
    return [(x * 2 + k, ((x + s) % n_x) * 2 + k) for x in range(n_x) for k in range(2)]


def core_swap(n_col):
    return [(c, c ^ 1) for c in range(n_col)]


def ring_gather(block, axis, n):
    i = lax.axis_index(axis)
    fwd = bwd = block
    by_off = {0: block}
    for step in range(1, n // 2 + 1):
        ahead = [(j, (j + 1) % n) for j in range(n)]
        behind = [(j, (j - 1) % n) for j in range(n)]
        if 2 * step == n:
            half = block.shape[-1] // 2
            from_behind = lax.ppermute(fwd[..., :half], axis, ahead)
            from_ahead = lax.ppermute(bwd[..., half:], axis, behind)
            by_off[step] = jnp.concatenate([from_behind, from_ahead], axis=-1)
        else:
            fwd = lax.ppermute(fwd, axis, ahead)
            bwd = lax.ppermute(bwd, axis, behind)
            by_off[-step % n] = fwd
            by_off[step] = bwd
    stacked = jnp.stack([by_off[d] for d in range(n)], axis=0)
    return jnp.roll(stacked, i, axis=0)


def make_per_device(n_col, n_z, n_y):
    n_x = n_col // 2

    def per_device(saved_input, out_grad, weight):
        c = lax.axis_index(COL)
        x = c // 2
        k = c % 2

        got = [saved_input]
        for s in range(1, n_x):
            got.append(lax.ppermute(saved_input, COL, chip_shift(n_col, s)))
        by_chip = jnp.stack(got, axis=0)
        order = (x - jnp.arange(n_x)) % n_x
        mine_by_x = jnp.take(by_chip, order, axis=0)
        other_by_x = lax.ppermute(mine_by_x, COL, core_swap(n_col))
        pair = jnp.where(k == 0, jnp.stack([mine_by_x, other_by_x], axis=1),
                         jnp.stack([other_by_x, mine_by_x], axis=1))
        saved_all = pair.reshape((n_col * saved_input.shape[0], saved_input.shape[1]))

        tokens = out_grad.shape[0] * n_z * n_y
        zg = ring_gather(out_grad, "z", n_z)
        y = lax.axis_index("y")
        ahead = [(j, (j + 1) % n_y) for j in range(n_y)]
        behind = [(j, (j - 1) % n_y) for j in range(n_y)]
        from_behind = lax.ppermute(zg, "y", ahead)
        from_ahead = lax.ppermute(zg, "y", behind)
        cut = zg.shape[-1] // 2
        far = jnp.concatenate([lax.ppermute(from_behind[..., :cut], "y", ahead),
                               lax.ppermute(from_ahead[..., cut:], "y", behind)], axis=-1)
        saved_all, from_behind, from_ahead = lax.optimization_barrier(
            (saved_all, from_behind, from_ahead))
        by_off = {0: zg, 1: from_ahead, n_y - 1: from_behind, 2: far}
        gathered = jnp.roll(jnp.stack([by_off[d] for d in range(n_y)], axis=0), y, axis=0)
        grad_all = gathered.reshape((tokens, out_grad.shape[1]))
        rows_r = out_grad.shape[0]


        gelu_value, unused_slope = gelu_parts(saved_all.astype(jnp.float32))
        hidden = gelu_value.astype(jnp.bfloat16).reshape((n_z, n_y, rows_r, -1))
        hidden = jnp.swapaxes(hidden, 0, 1)
        weight_grad = None
        for d in range(n_y):
            term = lax.dot_general(
                lax.dynamic_index_in_dim(hidden, (y + d) % n_y, axis=0, keepdims=False),
                by_off[d], (((0, 1), (0, 1)), ((), ())), preferred_element_type=jnp.float32)
            weight_grad = term if weight_grad is None else weight_grad + term
        weight_grad = weight_grad.astype(jnp.bfloat16)

        rows = saved_input.shape[0]
        if n_z == n_col:
            g = grad_all.reshape((n_y, n_x, 2, rows_r, -1))
            g_theirs = lax.dynamic_index_in_dim(g, 1 - k, axis=2, keepdims=False)
            g_mine = lax.dynamic_index_in_dim(g, k, axis=2, keepdims=False)
            p_theirs = lax.dot_general(g_theirs, weight, (((3,), (1,)), ((), ())),
                                       preferred_element_type=jnp.float32)
            got_theirs = lax.ppermute(p_theirs.astype(jnp.bfloat16), COL, core_swap(n_col))
            p_mine = lax.dot_general(g_mine, weight, (((3,), (1,)), ((), ())),
                                     preferred_element_type=jnp.float32)
            chip_sum = p_mine + got_theirs.astype(jnp.float32)
            pick = lambda c: lax.dynamic_index_in_dim(
                chip_sum, c, axis=1, keepdims=False).reshape((rows, -1))
        else:
            partial = lax.dot_general(
                grad_all, weight, (((1,), (1,)), ((), ())), preferred_element_type=jnp.float32
            )
            p_nat = jnp.swapaxes(partial.reshape((n_y, n_z, rows_r, -1)), 0, 1)
            p4 = p_nat.reshape((n_x, 2, rows, partial.shape[1]))
            mine = lax.dynamic_index_in_dim(p4, k, axis=1, keepdims=False)
            theirs = lax.dynamic_index_in_dim(p4, 1 - k, axis=1, keepdims=False)
            chip_sum = mine + lax.ppermute(theirs, COL, core_swap(n_col))
            pick = lambda c: lax.dynamic_index_in_dim(chip_sum, c, axis=0, keepdims=False)
        back = pick(x)
        dest = lambda s: pick((x + s) % n_x).astype(jnp.bfloat16)
        if n_x == 4:
            cut = back.shape[-1] // 2
            far = dest(2)
            up, up_relay = lax.ppermute((dest(1), far[:, :cut]), COL, chip_shift(n_col, 1))
            dn, dn_relay = lax.ppermute((dest(-1), far[:, cut:]), COL, chip_shift(n_col, -1))
            far_lo = lax.ppermute(up_relay, COL, chip_shift(n_col, 1))
            far_hi = lax.ppermute(dn_relay, COL, chip_shift(n_col, -1))
            far_got = jnp.concatenate([far_lo, far_hi], axis=-1)
            for recv in (up, dn, far_got):
                back = back + recv.astype(jnp.float32)
        else:
            for s in range(1, n_x):
                recv = lax.ppermute(dest(s), COL, chip_shift(n_col, s))
                back = back + recv.astype(jnp.float32)

        unused_value, own_slope = gelu_parts(saved_input.astype(jnp.float32))
        in_grad = (back * own_slope).astype(jnp.bfloat16)
        return (in_grad, weight_grad)

    return per_device


def solution(mesh):
    n_row, n_col = mesh.shape["row"], mesh.shape["col"]
    grid = Mesh(mesh.devices.reshape(n_row // 4, 4, n_col // 2, 2), ("z", "y", "x", "c"))
    row = ("z", "y")
    in_specs = (P(COL, row), P(row, COL), P(row, COL))
    out_specs = (P(COL, row), P(row, COL))
    return jax.shard_map(
        make_per_device(n_col, n_row // 4, 4),
        mesh=grid, in_specs=in_specs, out_specs=out_specs, check_vma=False,
    )
```

```python
import math

import jax
import jax.numpy as jnp
from jax import lax
from jax.sharding import Mesh, PartitionSpec as P

COL = ("x", "c")


def gelu_parts(values):
    coeff = math.sqrt(2.0 / math.pi)
    inner = jnp.tanh(coeff * (values + 0.044715 * values * values * values))
    gelu_value = 0.5 * values * (1.0 + inner)
    gelu_slope = 0.5 * (1.0 + inner) + 0.5 * values * (1.0 - inner * inner) * coeff * (
        1.0 + 3.0 * 0.044715 * values * values
    )
    return (gelu_value, gelu_slope)


def chip_shift(n_col, s):
    n_x = n_col // 2
    return [(x * 2 + k, ((x + s) % n_x) * 2 + k) for x in range(n_x) for k in range(2)]


def core_swap(n_col):
    return [(c, c ^ 1) for c in range(n_col)]


def ring_steps(block, axis, n):
    fwd = bwd = block
    by_off = {0: block}
    for step in range(1, n // 2 + 1):
        if 2 * step == n:
            half = block.shape[-1] // 2
            got = yield [(axis, 1, fwd[..., :half]), (axis, -1, bwd[..., half:])]
            by_off[step] = jnp.concatenate(got, axis=-1)
        else:
            fwd, bwd = yield [(axis, 1, fwd), (axis, -1, bwd)]
            by_off[-step % n] = fwd
            by_off[step] = bwd
    stacked = jnp.stack([by_off[d] for d in range(n)], axis=0)
    return jnp.roll(stacked, lax.axis_index(axis), axis=0)


def two_stage(block, first, second, sizes):
    inner = yield from ring_steps(block, first, sizes[first])
    return (yield from ring_steps(inner, second, sizes[second]))


def run_rings(jobs, sizes):
    results = [None] * len(jobs)
    asks = {}
    for j, job in enumerate(jobs):
        try:
            asks[j] = next(job)
        except StopIteration as done:
            results[j] = done.value
    while asks:
        groups = {}
        for j, ask in asks.items():
            for slot, (axis, step, value) in enumerate(ask):
                groups.setdefault((axis, step), []).append((j, slot, value))
        got = {j: [None] * len(ask) for j, ask in asks.items()}
        for (axis, step), items in groups.items():
            n = sizes[axis]
            perm = [(i, (i + step) % n) for i in range(n)]
            flat = [v.reshape(-1) for _, _, v in items]
            sent = lax.ppermute(jnp.concatenate(flat) if len(flat) > 1 else flat[0], axis, perm)
            at = 0
            for j, slot, value in items:
                got[j][slot] = sent[at:at + value.size].reshape(value.shape)
                at += value.size
        nxt = {}
        for j in asks:
            try:
                nxt[j] = jobs[j].send(got[j])
            except StopIteration as done:
                results[j] = done.value
        asks = nxt
    return results


def make_per_device(n_col, n_z, n_y):
    n_x = n_col // 2

    def per_device(saved_input, out_grad, weight):
        c = lax.axis_index(COL)
        x = c // 2
        k = c % 2

        tokens = out_grad.shape[0] * n_z * n_y
        sizes = {"z": n_z, "y": n_y}
        half = out_grad.shape[1] // 2
        part_a, part_b = run_rings(
            [two_stage(out_grad[:, :half], "z", "y", sizes),
             two_stage(out_grad[:, half:], "y", "z", sizes)], sizes)
        part_b = jnp.swapaxes(part_b, 0, 1)
        grad_all = jnp.concatenate([part_a, part_b], axis=-1).reshape((tokens, out_grad.shape[1]))
        rows_r = out_grad.shape[0]

        got = [saved_input]
        for s in range(1, n_x):
            got.append(lax.ppermute(saved_input, COL, chip_shift(n_col, s)))
        by_chip = jnp.stack(got, axis=0)
        order = (x - jnp.arange(n_x)) % n_x
        mine_by_x = jnp.take(by_chip, order, axis=0)
        other_by_x = lax.ppermute(mine_by_x, COL, core_swap(n_col))
        pair = jnp.where(k == 0, jnp.stack([mine_by_x, other_by_x], axis=1),
                         jnp.stack([other_by_x, mine_by_x], axis=1))
        saved_all = pair.reshape((n_col * saved_input.shape[0], saved_input.shape[1]))

        saved_all, grad_all = lax.optimization_barrier((saved_all, grad_all))
        gelu_value, unused_slope = gelu_parts(saved_all.astype(jnp.float32))
        hidden = gelu_value.astype(jnp.bfloat16).reshape((n_z, n_y, rows_r, -1))
        hidden = jnp.swapaxes(hidden, 0, 1).reshape((tokens, -1))
        weight_grad = lax.dot_general(
            hidden, grad_all, (((0,), (0,)), ((), ())), preferred_element_type=jnp.float32
        ).astype(jnp.bfloat16)

        rows = saved_input.shape[0]
        if n_z == n_col:
            g = grad_all.reshape((n_y, n_x, 2, rows_r, -1))
            g_theirs = lax.dynamic_index_in_dim(g, 1 - k, axis=2, keepdims=False)
            g_mine = lax.dynamic_index_in_dim(g, k, axis=2, keepdims=False)
            p_theirs = lax.dot_general(g_theirs, weight, (((3,), (1,)), ((), ())),
                                       preferred_element_type=jnp.float32)
            got_theirs = lax.ppermute(p_theirs.astype(jnp.bfloat16), COL, core_swap(n_col))
            p_mine = lax.dot_general(g_mine, weight, (((3,), (1,)), ((), ())),
                                     preferred_element_type=jnp.float32)
            chip_sum = p_mine + got_theirs.astype(jnp.float32)
            pick = lambda c: lax.dynamic_index_in_dim(
                chip_sum, c, axis=1, keepdims=False).reshape((rows, -1))
        else:
            partial = lax.dot_general(
                grad_all, weight, (((1,), (1,)), ((), ())), preferred_element_type=jnp.float32
            )
            p_nat = jnp.swapaxes(partial.reshape((n_y, n_z, rows_r, -1)), 0, 1)
            p4 = p_nat.reshape((n_x, 2, rows, partial.shape[1]))
            mine = lax.dynamic_index_in_dim(p4, k, axis=1, keepdims=False)
            theirs = lax.dynamic_index_in_dim(p4, 1 - k, axis=1, keepdims=False)
            chip_sum = mine + lax.ppermute(theirs, COL, core_swap(n_col))
            pick = lambda c: lax.dynamic_index_in_dim(chip_sum, c, axis=0, keepdims=False)
        back = pick(x)
        dest = lambda s: pick((x + s) % n_x).astype(jnp.bfloat16)
        if n_x == 4:
            cut = back.shape[-1] // 2
            far = dest(2)
            up, up_relay = lax.ppermute((dest(1), far[:, :cut]), COL, chip_shift(n_col, 1))
            dn, dn_relay = lax.ppermute((dest(-1), far[:, cut:]), COL, chip_shift(n_col, -1))
            far_lo = lax.ppermute(up_relay, COL, chip_shift(n_col, 1))
            far_hi = lax.ppermute(dn_relay, COL, chip_shift(n_col, -1))
            far_got = jnp.concatenate([far_lo, far_hi], axis=-1)
            for recv in (up, dn, far_got):
                back = back + recv.astype(jnp.float32)
        else:
            for s in range(1, n_x):
                recv = lax.ppermute(dest(s), COL, chip_shift(n_col, s))
                back = back + recv.astype(jnp.float32)

        unused_value, own_slope = gelu_parts(saved_input.astype(jnp.float32))
        in_grad = (back * own_slope).astype(jnp.bfloat16)
        return (in_grad, weight_grad)

    return per_device


def solution(mesh):
    n_row, n_col = mesh.shape["row"], mesh.shape["col"]
    grid = Mesh(mesh.devices.reshape(n_row // 4, 4, n_col // 2, 2), ("z", "y", "x", "c"))
    row = ("z", "y")
    in_specs = (P(COL, row), P(row, COL), P(row, COL))
    out_specs = (P(COL, row), P(row, COL))
    return jax.shard_map(
        make_per_device(n_col, n_row // 4, 4),
        mesh=grid, in_specs=in_specs, out_specs=out_specs, check_vma=False,
    )
```

```python
import math

import jax
import jax.numpy as jnp
from jax import lax
from jax.sharding import Mesh, PartitionSpec as P

COL = ("x", "c")


def gelu_parts(values):
    coeff = math.sqrt(2.0 / math.pi)
    inner = jnp.tanh(coeff * (values + 0.044715 * values * values * values))
    gelu_value = 0.5 * values * (1.0 + inner)
    gelu_slope = 0.5 * (1.0 + inner) + 0.5 * values * (1.0 - inner * inner) * coeff * (
        1.0 + 3.0 * 0.044715 * values * values
    )
    return (gelu_value, gelu_slope)


def chip_shift(n_col, s):
    n_x = n_col // 2
    return [(x * 2 + k, ((x + s) % n_x) * 2 + k) for x in range(n_x) for k in range(2)]


def core_swap(n_col):
    return [(c, c ^ 1) for c in range(n_col)]


def ring_gather(block, axis, n):
    i = lax.axis_index(axis)
    fwd = bwd = block
    by_off = {0: block}
    for step in range(1, n // 2 + 1):
        ahead = [(j, (j + 1) % n) for j in range(n)]
        behind = [(j, (j - 1) % n) for j in range(n)]
        if 2 * step == n:
            half = block.shape[-1] // 2
            from_behind = lax.ppermute(fwd[..., :half], axis, ahead)
            from_ahead = lax.ppermute(bwd[..., half:], axis, behind)
            by_off[step] = jnp.concatenate([from_behind, from_ahead], axis=-1)
        else:
            fwd = lax.ppermute(fwd, axis, ahead)
            bwd = lax.ppermute(bwd, axis, behind)
            by_off[-step % n] = fwd
            by_off[step] = bwd
    stacked = jnp.stack([by_off[d] for d in range(n)], axis=0)
    return jnp.roll(stacked, i, axis=0)


def z_then_y(block, n_z, n_y):
    z = lax.axis_index("z")
    fwd = bwd = block
    by_off = {0: block}
    groups, taken = [], set()
    mid = max(1, n_z // 4)
    for step in range(1, n_z // 2 + 1):
        ahead = [(j, (j + 1) % n_z) for j in range(n_z)]
        behind = [(j, (j - 1) % n_z) for j in range(n_z)]
        if 2 * step == n_z:
            half = block.shape[-1] // 2
            by_off[step] = jnp.concatenate([lax.ppermute(fwd[..., :half], "z", ahead),
                                            lax.ppermute(bwd[..., half:], "z", behind)], axis=-1)
        else:
            fwd = lax.ppermute(fwd, "z", ahead)
            bwd = lax.ppermute(bwd, "z", behind)
            by_off[-step % n_z] = fwd
            by_off[step] = bwd
        if step == mid or step == n_z // 2:
            new = [d for d in sorted(by_off) if d not in taken]
            taken.update(new)
            groups.append(new)
    if not groups:
        groups.append([0])
    parts = [ring_gather(jnp.stack([by_off[d] for d in g], axis=0), "y", n_y) for g in groups]
    offsets = [d for g in groups for d in g]
    joined = jnp.concatenate(parts, axis=1)
    where = jnp.array([offsets.index(d) for d in range(n_z)], dtype=jnp.int32)
    pick = jnp.take(where, (jnp.arange(n_z) - z) % n_z)
    return jnp.take(joined, pick, axis=1)


def make_per_device(n_col, n_z, n_y):
    n_x = n_col // 2

    def per_device(saved_input, out_grad, weight):
        c = lax.axis_index(COL)
        x = c // 2
        k = c % 2

        tokens = out_grad.shape[0] * n_z * n_y
        gathered = z_then_y(out_grad, n_z, n_y)
        grad_all = gathered.reshape((tokens, out_grad.shape[1]))
        rows_r = out_grad.shape[0]

        got = [saved_input]
        for s in range(1, n_x):
            got.append(lax.ppermute(saved_input, COL, chip_shift(n_col, s)))
        by_chip = jnp.stack(got, axis=0)
        order = (x - jnp.arange(n_x)) % n_x
        mine_by_x = jnp.take(by_chip, order, axis=0)
        other_by_x = lax.ppermute(mine_by_x, COL, core_swap(n_col))
        pair = jnp.where(k == 0, jnp.stack([mine_by_x, other_by_x], axis=1),
                         jnp.stack([other_by_x, mine_by_x], axis=1))
        saved_all = pair.reshape((n_col * saved_input.shape[0], saved_input.shape[1]))

        saved_all, grad_all = lax.optimization_barrier((saved_all, grad_all))
        gelu_value, unused_slope = gelu_parts(saved_all.astype(jnp.float32))
        hidden = gelu_value.astype(jnp.bfloat16).reshape((n_z, n_y, rows_r, -1))
        hidden = jnp.swapaxes(hidden, 0, 1).reshape((tokens, -1))
        weight_grad = lax.dot_general(
            hidden, grad_all, (((0,), (0,)), ((), ())), preferred_element_type=jnp.float32
        ).astype(jnp.bfloat16)

        rows = saved_input.shape[0]
        if n_z == n_col:
            g = grad_all.reshape((n_y, n_x, 2, rows_r, -1))
            g_theirs = lax.dynamic_index_in_dim(g, 1 - k, axis=2, keepdims=False)
            g_mine = lax.dynamic_index_in_dim(g, k, axis=2, keepdims=False)
            p_theirs = lax.dot_general(g_theirs, weight, (((3,), (1,)), ((), ())),
                                       preferred_element_type=jnp.float32)
            got_theirs = lax.ppermute(p_theirs.astype(jnp.bfloat16), COL, core_swap(n_col))
            p_mine = lax.dot_general(g_mine, weight, (((3,), (1,)), ((), ())),
                                     preferred_element_type=jnp.float32)
            chip_sum = p_mine + got_theirs.astype(jnp.float32)
            pick = lambda c: lax.dynamic_index_in_dim(
                chip_sum, c, axis=1, keepdims=False).reshape((rows, -1))
        else:
            partial = lax.dot_general(
                grad_all, weight, (((1,), (1,)), ((), ())), preferred_element_type=jnp.float32
            )
            p_nat = jnp.swapaxes(partial.reshape((n_y, n_z, rows_r, -1)), 0, 1)
            p4 = p_nat.reshape((n_x, 2, rows, partial.shape[1]))
            mine = lax.dynamic_index_in_dim(p4, k, axis=1, keepdims=False)
            theirs = lax.dynamic_index_in_dim(p4, 1 - k, axis=1, keepdims=False)
            chip_sum = mine + lax.ppermute(theirs, COL, core_swap(n_col))
            pick = lambda c: lax.dynamic_index_in_dim(chip_sum, c, axis=0, keepdims=False)
        back = pick(x)
        dest = lambda s: pick((x + s) % n_x).astype(jnp.bfloat16)
        if n_x == 4:
            cut = back.shape[-1] // 2
            far = dest(2)
            up, up_relay = lax.ppermute((dest(1), far[:, :cut]), COL, chip_shift(n_col, 1))
            dn, dn_relay = lax.ppermute((dest(-1), far[:, cut:]), COL, chip_shift(n_col, -1))
            far_lo = lax.ppermute(up_relay, COL, chip_shift(n_col, 1))
            far_hi = lax.ppermute(dn_relay, COL, chip_shift(n_col, -1))
            far_got = jnp.concatenate([far_lo, far_hi], axis=-1)
            for recv in (up, dn, far_got):
                back = back + recv.astype(jnp.float32)
        else:
            for s in range(1, n_x):
                recv = lax.ppermute(dest(s), COL, chip_shift(n_col, s))
                back = back + recv.astype(jnp.float32)

        unused_value, own_slope = gelu_parts(saved_input.astype(jnp.float32))
        in_grad = (back * own_slope).astype(jnp.bfloat16)
        return (in_grad, weight_grad)

    return per_device


def solution(mesh):
    n_row, n_col = mesh.shape["row"], mesh.shape["col"]
    grid = Mesh(mesh.devices.reshape(n_row // 4, 4, n_col // 2, 2), ("z", "y", "x", "c"))
    row = ("z", "y")
    in_specs = (P(COL, row), P(row, COL), P(row, COL))
    out_specs = (P(COL, row), P(row, COL))
    return jax.shard_map(
        make_per_device(n_col, n_row // 4, 4),
        mesh=grid, in_specs=in_specs, out_specs=out_specs, check_vma=False,
    )
```

```python
import math

import jax
import jax.numpy as jnp
from jax import lax
from jax.sharding import Mesh, PartitionSpec as P

COL = ("x", "c")


def gelu_parts(values):
    coeff = math.sqrt(2.0 / math.pi)
    inner = jnp.tanh(coeff * (values + 0.044715 * values * values * values))
    gelu_value = 0.5 * values * (1.0 + inner)
    gelu_slope = 0.5 * (1.0 + inner) + 0.5 * values * (1.0 - inner * inner) * coeff * (
        1.0 + 3.0 * 0.044715 * values * values
    )
    return (gelu_value, gelu_slope)


def chip_shift(n_col, s):
    n_x = n_col // 2
    return [(x * 2 + k, ((x + s) % n_x) * 2 + k) for x in range(n_x) for k in range(2)]


def core_swap(n_col):
    return [(c, c ^ 1) for c in range(n_col)]


def ring_gather(block, axis, n):
    i = lax.axis_index(axis)
    fwd = bwd = block
    by_off = {0: block}
    for step in range(1, n // 2 + 1):
        ahead = [(j, (j + 1) % n) for j in range(n)]
        behind = [(j, (j - 1) % n) for j in range(n)]
        if 2 * step == n:
            half = block.shape[-1] // 2
            from_behind = lax.ppermute(fwd[..., :half], axis, ahead)
            from_ahead = lax.ppermute(bwd[..., half:], axis, behind)
            by_off[step] = jnp.concatenate([from_behind, from_ahead], axis=-1)
        else:
            fwd = lax.ppermute(fwd, axis, ahead)
            bwd = lax.ppermute(bwd, axis, behind)
            by_off[-step % n] = fwd
            by_off[step] = bwd
    arrival = [0]
    for step in range(1, n // 2 + 1):
        arrival += [d for d in (-step % n, step) if d not in arrival]
    out = jnp.zeros((n,) + block.shape, block.dtype)
    for d in arrival:
        out = lax.dynamic_update_slice_in_dim(out, by_off[d][None], (i + d) % n, axis=0)
    return out


def make_per_device(n_col, n_z, n_y):
    n_x = n_col // 2

    def per_device(saved_input, out_grad, weight):
        c = lax.axis_index(COL)
        x = c // 2
        k = c % 2

        tokens = out_grad.shape[0] * n_z * n_y
        gathered = ring_gather(ring_gather(out_grad, "z", n_z), "y", n_y)
        grad_all = gathered.reshape((tokens, out_grad.shape[1]))
        rows_r = out_grad.shape[0]

        got = [saved_input]
        for s in range(1, n_x):
            got.append(lax.ppermute(saved_input, COL, chip_shift(n_col, s)))
        by_chip = jnp.stack(got, axis=0)
        order = (x - jnp.arange(n_x)) % n_x
        mine_by_x = jnp.take(by_chip, order, axis=0)
        other_by_x = lax.ppermute(mine_by_x, COL, core_swap(n_col))
        pair = jnp.where(k == 0, jnp.stack([mine_by_x, other_by_x], axis=1),
                         jnp.stack([other_by_x, mine_by_x], axis=1))
        saved_all = pair.reshape((n_col * saved_input.shape[0], saved_input.shape[1]))

        saved_all, grad_all = lax.optimization_barrier((saved_all, grad_all))
        gelu_value, unused_slope = gelu_parts(saved_all.astype(jnp.float32))
        hidden = gelu_value.astype(jnp.bfloat16).reshape((n_z, n_y, rows_r, -1))
        hidden = jnp.swapaxes(hidden, 0, 1).reshape((tokens, -1))
        weight_grad = lax.dot_general(
            hidden, grad_all, (((0,), (0,)), ((), ())), preferred_element_type=jnp.float32
        ).astype(jnp.bfloat16)

        rows = saved_input.shape[0]
        if n_z == n_col:
            g = grad_all.reshape((n_y, n_x, 2, rows_r, -1))
            g_theirs = lax.dynamic_index_in_dim(g, 1 - k, axis=2, keepdims=False)
            g_mine = lax.dynamic_index_in_dim(g, k, axis=2, keepdims=False)
            p_theirs = lax.dot_general(g_theirs, weight, (((3,), (1,)), ((), ())),
                                       preferred_element_type=jnp.float32)
            got_theirs = lax.ppermute(p_theirs.astype(jnp.bfloat16), COL, core_swap(n_col))
            p_mine = lax.dot_general(g_mine, weight, (((3,), (1,)), ((), ())),
                                     preferred_element_type=jnp.float32)
            chip_sum = p_mine + got_theirs.astype(jnp.float32)
            pick = lambda c: lax.dynamic_index_in_dim(
                chip_sum, c, axis=1, keepdims=False).reshape((rows, -1))
        else:
            partial = lax.dot_general(
                grad_all, weight, (((1,), (1,)), ((), ())), preferred_element_type=jnp.float32
            )
            p_nat = jnp.swapaxes(partial.reshape((n_y, n_z, rows_r, -1)), 0, 1)
            p4 = p_nat.reshape((n_x, 2, rows, partial.shape[1]))
            mine = lax.dynamic_index_in_dim(p4, k, axis=1, keepdims=False)
            theirs = lax.dynamic_index_in_dim(p4, 1 - k, axis=1, keepdims=False)
            chip_sum = mine + lax.ppermute(theirs, COL, core_swap(n_col))
            pick = lambda c: lax.dynamic_index_in_dim(chip_sum, c, axis=0, keepdims=False)
        back = pick(x)
        dest = lambda s: pick((x + s) % n_x).astype(jnp.bfloat16)
        if n_x == 4:
            cut = back.shape[-1] // 2
            far = dest(2)
            up, up_relay = lax.ppermute((dest(1), far[:, :cut]), COL, chip_shift(n_col, 1))
            dn, dn_relay = lax.ppermute((dest(-1), far[:, cut:]), COL, chip_shift(n_col, -1))
            far_lo = lax.ppermute(up_relay, COL, chip_shift(n_col, 1))
            far_hi = lax.ppermute(dn_relay, COL, chip_shift(n_col, -1))
            far_got = jnp.concatenate([far_lo, far_hi], axis=-1)
            for recv in (up, dn, far_got):
                back = back + recv.astype(jnp.float32)
        else:
            for s in range(1, n_x):
                recv = lax.ppermute(dest(s), COL, chip_shift(n_col, s))
                back = back + recv.astype(jnp.float32)

        unused_value, own_slope = gelu_parts(saved_input.astype(jnp.float32))
        in_grad = (back * own_slope).astype(jnp.bfloat16)
        return (in_grad, weight_grad)

    return per_device


def solution(mesh):
    n_row, n_col = mesh.shape["row"], mesh.shape["col"]
    grid = Mesh(mesh.devices.reshape(n_row // 4, 4, n_col // 2, 2), ("z", "y", "x", "c"))
    row = ("z", "y")
    in_specs = (P(COL, row), P(row, COL), P(row, COL))
    out_specs = (P(COL, row), P(row, COL))
    return jax.shard_map(
        make_per_device(n_col, n_row // 4, 4),
        mesh=grid, in_specs=in_specs, out_specs=out_specs, check_vma=False,
    )
```

```python
import math

import jax
import jax.numpy as jnp
from jax import lax
from jax.sharding import Mesh, PartitionSpec as P

COL = ("x", "c")


def gelu_parts(values):
    coeff = math.sqrt(2.0 / math.pi)
    inner = jnp.tanh(coeff * (values + 0.044715 * values * values * values))
    gelu_value = 0.5 * values * (1.0 + inner)
    gelu_slope = 0.5 * (1.0 + inner) + 0.5 * values * (1.0 - inner * inner) * coeff * (
        1.0 + 3.0 * 0.044715 * values * values
    )
    return (gelu_value, gelu_slope)


def chip_shift(n_col, s):
    n_x = n_col // 2
    return [(x * 2 + k, ((x + s) % n_x) * 2 + k) for x in range(n_x) for k in range(2)]


def core_swap(n_col):
    return [(c, c ^ 1) for c in range(n_col)]


def ring_gather(block, axis, n):
    i = lax.axis_index(axis)
    fwd = bwd = block
    by_off = {0: block}
    for step in range(1, n // 2 + 1):
        ahead = [(j, (j + 1) % n) for j in range(n)]
        behind = [(j, (j - 1) % n) for j in range(n)]
        if 2 * step == n:
            half = block.shape[-1] // 2
            from_behind = lax.ppermute(fwd[..., :half], axis, ahead)
            from_ahead = lax.ppermute(bwd[..., half:], axis, behind)
            by_off[step] = jnp.concatenate([from_behind, from_ahead], axis=-1)
        else:
            fwd = lax.ppermute(fwd, axis, ahead)
            bwd = lax.ppermute(bwd, axis, behind)
            by_off[-step % n] = fwd
            by_off[step] = bwd
    arrival = [0]
    for step in range(1, n // 2 + 1):
        arrival += [d for d in (-step % n, step) if d not in arrival]
    out = jnp.zeros((n,) + block.shape, block.dtype)
    for d in arrival:
        out = lax.dynamic_update_slice_in_dim(out, by_off[d][None], (i + d) % n, axis=0)
    return out


def make_per_device(n_col, n_z, n_y):
    n_x = n_col // 2

    def per_device(saved_input, out_grad, weight):
        c = lax.axis_index(COL)
        x = c // 2
        k = c % 2

        tokens = out_grad.shape[0] * n_z * n_y
        gathered = ring_gather(ring_gather(out_grad, "z", n_z), "y", n_y)
        grad_all = gathered.reshape((tokens, out_grad.shape[1]))
        rows_r = out_grad.shape[0]

        got = [saved_input]
        for s in range(1, n_x):
            got.append(lax.ppermute(saved_input, COL, chip_shift(n_col, s)))
        by_chip = jnp.stack(got, axis=0)
        order = (x - jnp.arange(n_x)) % n_x
        mine_by_x = jnp.take(by_chip, order, axis=0)
        other_by_x = lax.ppermute(mine_by_x, COL, core_swap(n_col))
        pair = jnp.where(k == 0, jnp.stack([mine_by_x, other_by_x], axis=1),
                         jnp.stack([other_by_x, mine_by_x], axis=1))
        saved_all = pair.reshape((n_col * saved_input.shape[0], saved_input.shape[1]))

        saved_all, grad_all = lax.optimization_barrier((saved_all, grad_all))
        gelu_value, unused_slope = gelu_parts(saved_all.astype(jnp.float32))
        hidden = gelu_value.astype(jnp.bfloat16).reshape((n_z, n_y, rows_r, -1))
        hidden = jnp.swapaxes(hidden, 0, 1).reshape((tokens, -1))
        weight_grad = lax.dot_general(
            hidden, grad_all, (((0,), (0,)), ((), ())), preferred_element_type=jnp.float32
        ).astype(jnp.bfloat16)

        rows = saved_input.shape[0]
        if n_z == n_col:
            g = grad_all.reshape((n_y, n_x, 2, rows_r, -1))
            g_theirs = lax.dynamic_index_in_dim(g, 1 - k, axis=2, keepdims=False)
            g_mine = lax.dynamic_index_in_dim(g, k, axis=2, keepdims=False)
            p_theirs = lax.dot_general(g_theirs, weight, (((3,), (1,)), ((), ())),
                                       preferred_element_type=jnp.float32)
            got_theirs = lax.ppermute(p_theirs.astype(jnp.bfloat16), COL, core_swap(n_col))
            p_mine = lax.dot_general(g_mine, weight, (((3,), (1,)), ((), ())),
                                     preferred_element_type=jnp.float32)
            chip_sum = p_mine + got_theirs.astype(jnp.float32)
            pick = lambda c: lax.dynamic_index_in_dim(
                chip_sum, c, axis=1, keepdims=False).reshape((rows, -1))
        else:
            partial = lax.dot_general(
                grad_all, weight, (((1,), (1,)), ((), ())), preferred_element_type=jnp.float32
            )
            p_nat = jnp.swapaxes(partial.reshape((n_y, n_z, rows_r, -1)), 0, 1)
            p4 = p_nat.reshape((n_x, 2, rows, partial.shape[1]))
            mine = lax.dynamic_index_in_dim(p4, k, axis=1, keepdims=False)
            theirs = lax.dynamic_index_in_dim(p4, 1 - k, axis=1, keepdims=False)
            chip_sum = mine + lax.ppermute(theirs, COL, core_swap(n_col))
            pick = lambda c: lax.dynamic_index_in_dim(chip_sum, c, axis=0, keepdims=False)
        back = pick(x)
        dest = lambda s: pick((x + s) % n_x).astype(jnp.bfloat16)
        for s in range(1, n_x):
            recv = lax.ppermute(dest(s), COL, chip_shift(n_col, s))
            back = back + recv.astype(jnp.float32)

        unused_value, own_slope = gelu_parts(saved_input.astype(jnp.float32))
        in_grad = (back * own_slope).astype(jnp.bfloat16)
        return (in_grad, weight_grad)

    return per_device


def solution(mesh):
    n_row, n_col = mesh.shape["row"], mesh.shape["col"]
    grid = Mesh(mesh.devices.reshape(n_row // 4, 4, n_col // 2, 2), ("z", "y", "x", "c"))
    row = ("z", "y")
    in_specs = (P(COL, row), P(row, COL), P(row, COL))
    out_specs = (P(COL, row), P(row, COL))
    return jax.shard_map(
        make_per_device(n_col, n_row // 4, 4),
        mesh=grid, in_specs=in_specs, out_specs=out_specs, check_vma=False,
    )
```

```python
import math

import jax
import jax.numpy as jnp
from jax import lax
from jax.sharding import Mesh, PartitionSpec as P

COL = ("x", "c")


def gelu_parts(values):
    coeff = math.sqrt(2.0 / math.pi)
    inner = jnp.tanh(coeff * (values + 0.044715 * values * values * values))
    gelu_value = 0.5 * values * (1.0 + inner)
    gelu_slope = 0.5 * (1.0 + inner) + 0.5 * values * (1.0 - inner * inner) * coeff * (
        1.0 + 3.0 * 0.044715 * values * values
    )
    return (gelu_value, gelu_slope)


def chip_shift(n_col, s):
    n_x = n_col // 2
    return [(x * 2 + k, ((x + s) % n_x) * 2 + k) for x in range(n_x) for k in range(2)]


def core_swap(n_col):
    return [(c, c ^ 1) for c in range(n_col)]


def ring_gather(block, axis, n):
    i = lax.axis_index(axis)
    fwd = bwd = block
    by_off = {0: block}
    for step in range(1, n // 2 + 1):
        ahead = [(j, (j + 1) % n) for j in range(n)]
        behind = [(j, (j - 1) % n) for j in range(n)]
        if 2 * step == n:
            half = block.shape[-1] // 2
            from_behind = lax.ppermute(fwd[..., :half], axis, ahead)
            from_ahead = lax.ppermute(bwd[..., half:], axis, behind)
            by_off[step] = jnp.concatenate([from_behind, from_ahead], axis=-1)
        else:
            fwd = lax.ppermute(fwd, axis, ahead)
            bwd = lax.ppermute(bwd, axis, behind)
            by_off[-step % n] = fwd
            by_off[step] = bwd
    arrival = [0]
    for step in range(1, n // 2 + 1):
        arrival += [d for d in (-step % n, step) if d not in arrival]
    out = jnp.zeros((n,) + block.shape, block.dtype)
    for d in arrival:
        out = lax.dynamic_update_slice_in_dim(out, by_off[d][None], (i + d) % n, axis=0)
    return out


def make_per_device(n_col, n_z, n_y):
    n_x = n_col // 2

    def per_device(saved_input, out_grad, weight):
        c = lax.axis_index(COL)
        x = c // 2
        k = c % 2

        tokens = out_grad.shape[0] * n_z * n_y
        gathered = ring_gather(ring_gather(out_grad, "z", n_z), "y", n_y)
        grad_all = gathered.reshape((tokens, out_grad.shape[1]))
        rows_r = out_grad.shape[0]

        got = [saved_input]
        for s in range(1, n_x):
            got.append(lax.ppermute(saved_input, COL, chip_shift(n_col, s)))
        by_chip = jnp.stack(got, axis=0)
        order = (x - jnp.arange(n_x)) % n_x
        mine_by_x = jnp.take(by_chip, order, axis=0)
        other_by_x = lax.ppermute(mine_by_x, COL, core_swap(n_col))
        pair = jnp.where(k == 0, jnp.stack([mine_by_x, other_by_x], axis=1),
                         jnp.stack([other_by_x, mine_by_x], axis=1))
        saved_all = pair.reshape((n_col * saved_input.shape[0], saved_input.shape[1]))

        saved_all, grad_all = lax.optimization_barrier((saved_all, grad_all))
        gelu_value, unused_slope = gelu_parts(saved_all.astype(jnp.float32))
        hidden = gelu_value.astype(jnp.bfloat16).reshape((n_z, n_y, rows_r, -1))
        hidden = jnp.swapaxes(hidden, 0, 1).reshape((tokens, -1))
        weight_grad = lax.dot_general(
            hidden, grad_all, (((0,), (0,)), ((), ())), preferred_element_type=jnp.float32
        ).astype(jnp.bfloat16)

        rows = saved_input.shape[0]
        if n_z == n_col:
            g = grad_all.reshape((n_y, n_x, 2, rows_r, -1))
            g_theirs = lax.dynamic_index_in_dim(g, 1 - k, axis=2, keepdims=False)
            g_mine = lax.dynamic_index_in_dim(g, k, axis=2, keepdims=False)
            p_theirs = lax.dot_general(g_theirs, weight, (((3,), (1,)), ((), ())),
                                       preferred_element_type=jnp.float32)
            got_theirs = lax.ppermute(p_theirs.astype(jnp.bfloat16), COL, core_swap(n_col))
            p_mine = lax.dot_general(g_mine, weight, (((3,), (1,)), ((), ())),
                                     preferred_element_type=jnp.float32)
            chip_sum = p_mine + got_theirs.astype(jnp.float32)
            pick = lambda c: lax.dynamic_index_in_dim(
                chip_sum, c, axis=1, keepdims=False).reshape((rows, -1))
        else:
            partial = lax.dot_general(
                grad_all, weight, (((1,), (1,)), ((), ())), preferred_element_type=jnp.float32
            )
            p_nat = jnp.swapaxes(partial.reshape((n_y, n_z, rows_r, -1)), 0, 1)
            p4 = p_nat.reshape((n_x, 2, rows, partial.shape[1]))
            mine = lax.dynamic_index_in_dim(p4, k, axis=1, keepdims=False)
            theirs = lax.dynamic_index_in_dim(p4, 1 - k, axis=1, keepdims=False)
            chip_sum = mine + lax.ppermute(theirs, COL, core_swap(n_col))
            pick = lambda c: lax.dynamic_index_in_dim(chip_sum, c, axis=0, keepdims=False)
        back = pick(x)
        dest = lambda s: pick((x + s) % n_x).astype(jnp.bfloat16)
        for s in sorted(range(1, n_x), key=lambda s: -min(s, n_x - s)):
            recv = lax.ppermute(dest(s), COL, chip_shift(n_col, s))
            back = back + recv.astype(jnp.float32)

        unused_value, own_slope = gelu_parts(saved_input.astype(jnp.float32))
        in_grad = (back * own_slope).astype(jnp.bfloat16)
        return (in_grad, weight_grad)

    return per_device


def solution(mesh):
    n_row, n_col = mesh.shape["row"], mesh.shape["col"]
    grid = Mesh(mesh.devices.reshape(n_row // 4, 4, n_col // 2, 2), ("z", "y", "x", "c"))
    row = ("z", "y")
    in_specs = (P(COL, row), P(row, COL), P(row, COL))
    out_specs = (P(COL, row), P(row, COL))
    return jax.shard_map(
        make_per_device(n_col, n_row // 4, 4),
        mesh=grid, in_specs=in_specs, out_specs=out_specs, check_vma=False,
    )
```
